256 devices in a mesh: rep: 16 (over x_lo, y, core), shard: 16 (over z, x_hi).
Axes of the slice: x: 4 (x_hi: 2, x_lo: 2; x = x_hi * 2 + x_lo), y: 4, z: 8, core: 2. Of those that a mesh axis runs over, the one named last changes fastest.
Arguments:
- activations: bfloat16 [32768, 4096], P(('rep', 'shard')), may hold values from -24 to 24
- cotangent: bfloat16 [32768, 896], P(('rep', 'shard')), may hold values from -0.099609375 to 0.099609375
- weight: bfloat16 [16, 4096, 896], P('rep', 'shard'), may hold values from -6 to 6
- momentum: bfloat16 [16, 4096, 896], P('rep', 'shard'), may hold values from -6 to 6
- step_index: int32 [1], replicated, may hold values from 0 to 999
Outputs:
- averaged: bfloat16 [16, 4096, 896], P('rep', 'shard')
- momentum_new: bfloat16 [16, 4096, 896], P('rep', 'shard')
The draws below stay inside these ranges and needn't reach their ends.
All inputs are finite; a program needn't handle non-finite values.
Results may differ from the reference program's by a relative error of at most 0.012.
Values may be sent and summed in bfloat16 or wider, within the bound.
No kernel may reach another device: no remote copies, remote signals or barrier semaphores. Data moves between devices by JAX's collectives and lax.ppermute only.
A program may use at most 64 MiB of HBM per device.

```python
import jax
import jax.numpy as jnp
from jax import lax

D = 4096
HID = 448
TOK_DEV = 128
TOKENS = 32768
N_REP = 16
N_SHARD = 16


def raised(drawn, rng, source, target, shards_of, factor):
    def block_of(position):
        return (jnp.arange(drawn.shape[position]) // (drawn.shape[position] // shards_of)).reshape((-1,) + (1,) * (drawn.ndim - 1 - position))

    near = jax.random.permutation(rng, shards_of)[block_of(target)]
    far = (block_of(target) + shards_of // 2) % shards_of
    return jnp.where((block_of(source) == near) | (block_of(source) == far), factor * drawn, drawn)


def block_levels(own_key, shape, split, low, largest):
    loudness, own = 1.0, jax.random.fold_in(own_key, 6)
    for position, shards_of in split:
        steps = jnp.exp(jax.random.uniform(jax.random.fold_in(own, position), (shards_of,), jnp.float32, low / len(split), largest / len(split)))
        loudness = loudness * jnp.repeat(steps, shape[position] // shards_of).reshape([-1 if axis == position else 1 for axis in range(len(shape))])
    return loudness


def normal_values(stream_key, shape, spread, bound, shards=(), held_as=jnp.bfloat16):
    loudness = block_levels(stream_key, shape, shards, -0.22, 0.18) if shards else 1.0
    drawn = jax.random.normal(stream_key, shape, jnp.float32) * spread * loudness
    return jnp.minimum(jnp.maximum(drawn, -bound), bound).astype(held_as)


def bell_draw_with(stream_key, dims, width, bound, cuts, heavy, kind=jnp.bfloat16):
    array = width * jax.random.normal(stream_key, dims, jnp.float32)
    if cuts:
        array = array * block_levels(stream_key, dims, cuts, -0.22, 0.18)
    return jnp.clip(raised(array, jax.random.fold_in(stream_key, 3), *heavy), -bound, bound).astype(kind)


def setup_inputs(seed: int = 0) -> dict:
    key_of = jax.random.split(jax.random.key(seed), 6)
    return {
        "activations": bell_draw_with(key_of[0], (TOKENS, D), 1.0, 24.0, ((0, 256),), (0, 1, 256, 6.0)),
        "cotangent": normal_values(key_of[1], (TOKENS, 2 * HID), 0.015625, 0.099609375, ((0, 256),)),
        "weight": normal_values(key_of[2], (N_REP, D, 2 * HID), 1.0, 6.0, ((0, 16), (1, 16))),
        "momentum": normal_values(key_of[3], (N_REP, D, 2 * HID), 1.0, 6.0, ((0, 16), (1, 16))),
        "step_index": jax.random.randint(key_of[4], (1,), 0, 1000).astype(jnp.int32),
    }


def replica_gradient(paired):
    blocks_rows = paired[0].reshape(N_SHARD, TOK_DEV, D)
    blocks_cot = paired[1].reshape(N_SHARD, TOK_DEV, 2 * HID)

    def add_block(total, pair):
        part = jnp.dot(pair[0].T, pair[1], preferred_element_type=jnp.float32)
        rounded = lax.optimization_barrier(part.astype(jnp.bfloat16)).astype(jnp.float32)
        return total + rounded, None

    start = jnp.zeros((D, 2 * HID), jnp.float32)
    total, unused = lax.scan(add_block, start, (blocks_rows, blocks_cot))
    return total


def reference(activations, cotangent, weight, momentum, step_index):
    levels = N_REP.bit_length() - 1
    grouped_rows = activations.reshape(N_REP, N_SHARD * TOK_DEV, D)
    grouped_cot = cotangent.reshape(N_REP, N_SHARD * TOK_DEV, 2 * HID)
    gradient = lax.map(replica_gradient, (grouped_rows, grouped_cot))
    momentum_new = (0.9 * momentum.astype(jnp.float32) + gradient).astype(jnp.bfloat16)
    half_step = (weight.astype(jnp.float32) - 0.5 * momentum_new.astype(jnp.float32)).astype(jnp.bfloat16)
    distance = jnp.left_shift(jnp.int32(1), (step_index[0] % levels).astype(jnp.int32))
    source = ((jnp.arange(N_REP, dtype=jnp.int32) - distance) % N_REP).astype(jnp.int32)
    received = jnp.take(half_step, source, axis=0)
    averaged = (0.5 * (half_step.astype(jnp.float32) + received.astype(jnp.float32))).astype(jnp.bfloat16)
    return averaged, momentum_new
```

```python
import numpy as np
import jax
import jax.numpy as jnp
from jax import lax
from jax.sharding import Mesh, PartitionSpec as P

PAIR = 2


def shortened(value):

    def short(part):
        return part.astype(jnp.bfloat16) if part.dtype == jnp.float32 else part

    return jax.tree.map(short, value)


def from_behind(value, axis, by):
    count = lax.axis_size(axis)
    return lax.ppermute(value, axis, [(i, (i + by) % count) for i in range(count)])


def shifter(distance):
    return lambda tensor_value: jax.tree.map(
        lambda part, own: part.astype(own.dtype),
        from_behind(shortened(tensor_value), "rep", distance),
        tensor_value,
    )


def pair_gradient(activations, cotangent, rows):
    tokens, width = activations.shape
    nz = lax.axis_size("z")
    pair_rows = rows * PAIR
    columns = activations.reshape(tokens, nz, pair_rows).transpose(1, 0, 2)
    columns = lax.all_to_all(columns, "z", 0, 0)
    cot_blocks = lax.all_gather(cotangent, "z")
    partial = jnp.einsum(
        "ktr,ktc->krc", columns, cot_blocks, preferred_element_type=jnp.float32
    ).astype(jnp.bfloat16)
    return jnp.sum(partial.astype(jnp.float32), axis=0)


def per_device(activations, cotangent, weight, momentum, step_index):
    rows = weight.shape[1]
    pair_sum = pair_gradient(activations, cotangent, rows)
    side = lax.axis_index("xh")
    own = lax.dynamic_slice_in_dim(pair_sum, side * rows, rows, 0)
    other = lax.dynamic_slice_in_dim(pair_sum, (1 - side) * rows, rows, 0)
    swapped = lax.ppermute(other.astype(jnp.bfloat16), "xh", [(0, 1), (1, 0)])
    gradient = own + swapped.astype(jnp.float32)
    momentum_new = (0.9 * momentum[0].astype(jnp.float32) + gradient).astype(jnp.bfloat16)
    half_step = (weight[0].astype(jnp.float32) - 0.5 * momentum_new.astype(jnp.float32)).astype(
        jnp.bfloat16
    )
    levels = lax.axis_size("rep").bit_length() - 1
    branches = [shifter(1 << bit_number) for bit_number in range(levels)]
    received = lax.switch(step_index[0] % levels, branches, half_step)
    averaged = (0.5 * (half_step.astype(jnp.float32) + received.astype(jnp.float32))).astype(
        jnp.bfloat16
    )
    return (averaged[None], momentum_new[None])


def solution(mesh):
    n_rep, n_shard = mesh.devices.shape
    split = Mesh(
        np.asarray(mesh.devices).reshape(n_rep, n_shard // PAIR, PAIR), ("rep", "z", "xh")
    )
    tokens = ("rep", "z", "xh")
    return jax.shard_map(
        per_device,
        mesh=split,
        in_specs=(
            P(tokens, None),
            P(tokens, None),
            P("rep", ("z", "xh"), None),
            P("rep", ("z", "xh"), None),
            P(),
        ),
        out_specs=(P("rep", ("z", "xh"), None), P("rep", ("z", "xh"), None)),
        check_vma=False,
    )
```

```python
import numpy as np
import jax
import jax.numpy as jnp
from jax import lax
from jax.sharding import Mesh, PartitionSpec as P

PAIR = 2


def from_behind(value, axis, by):
    count = lax.axis_size(axis)
    return lax.ppermute(value, axis, [(i, (i + by) % count) for i in range(count)])


def pair_gradient(activations, cotangent, rows):
    tokens, width = activations.shape
    nz = lax.axis_size("z")
    pair_rows = rows * PAIR
    columns = activations.reshape(tokens, nz, pair_rows).transpose(1, 0, 2)
    columns = lax.all_to_all(columns, "z", 0, 0)
    cot_blocks = lax.all_gather(cotangent, "z")
    partial = jnp.einsum(
        "ktr,ktc->krc", columns, cot_blocks, preferred_element_type=jnp.float32
    ).astype(jnp.bfloat16)
    return jnp.sum(partial.astype(jnp.float32), axis=0)


def from_behind_across(value, distance):
    n_rep, n_side = lax.axis_size("rep"), lax.axis_size("xh")
    pairs = [
        (r * n_side + j, ((r + distance) % n_rep) * n_side + (n_side - 1 - j))
        for r in range(n_rep)
        for j in range(n_side)
    ]
    return lax.ppermute(value, ("rep", "xh"), pairs)


def tail_sends(distance):
    def run(own, other):
        swapped = lax.ppermute(other, "xh", [(0, 1), (1, 0)])
        return swapped, from_behind(own, "rep", distance), from_behind_across(other, distance)

    return run


def per_device(activations, cotangent, weight, momentum, step_index):
    rows = weight.shape[1]
    levels = lax.axis_size("rep").bit_length() - 1
    choice = step_index[0] % levels
    distances = [1 << bit_number for bit_number in range(levels)]
    held = jnp.stack([weight[0], momentum[0]])
    partner = lax.switch(
        choice, [lambda v, by=by: from_behind(v, "rep", by) for by in distances], held
    )
    pair_sum = pair_gradient(activations, cotangent, rows)
    side = lax.axis_index("xh")
    own = lax.dynamic_slice_in_dim(pair_sum, side * rows, rows, 0)
    other = lax.dynamic_slice_in_dim(pair_sum, (1 - side) * rows, rows, 0).astype(jnp.bfloat16)
    swapped, partner_own, partner_other = lax.switch(
        choice, [tail_sends(by) for by in distances], own.astype(jnp.bfloat16), other
    )

    def step(w, m, gradient):
        moment = (0.9 * m.astype(jnp.float32) + gradient).astype(jnp.bfloat16)
        half = (w.astype(jnp.float32) - 0.5 * moment.astype(jnp.float32)).astype(jnp.bfloat16)
        return moment, half

    momentum_new, half_step = step(weight[0], momentum[0], own + swapped.astype(jnp.float32))
    unused, received = step(
        partner[0],
        partner[1],
        partner_own.astype(jnp.float32) + partner_other.astype(jnp.float32),
    )
    averaged = (0.5 * (half_step.astype(jnp.float32) + received.astype(jnp.float32))).astype(
        jnp.bfloat16
    )
    return (averaged[None], momentum_new[None])


def solution(mesh):
    n_rep, n_shard = mesh.devices.shape
    split = Mesh(
        np.asarray(mesh.devices).reshape(n_rep, n_shard // PAIR, PAIR), ("rep", "z", "xh")
    )
    tokens = ("rep", "z", "xh")
    return jax.shard_map(
        per_device,
        mesh=split,
        in_specs=(
            P(tokens, None),
            P(tokens, None),
            P("rep", ("z", "xh"), None),
            P("rep", ("z", "xh"), None),
            P(),
        ),
        out_specs=(P("rep", ("z", "xh"), None), P("rep", ("z", "xh"), None)),
        check_vma=False,
    )
```

```python
import numpy as np
import jax
import jax.numpy as jnp
from jax import lax
from jax.sharding import Mesh, PartitionSpec as P

PAIR = 2


def shortened(value):

    def short(part):
        return part.astype(jnp.bfloat16) if part.dtype == jnp.float32 else part

    return jax.tree.map(short, value)


def from_behind(value, axis, by):
    count = lax.axis_size(axis)
    return lax.ppermute(value, axis, [(i, (i + by) % count) for i in range(count)])


def shifter(distance):
    return lambda tensor_value: jax.tree.map(
        lambda part, own: part.astype(own.dtype),
        from_behind(shortened(tensor_value), "rep", distance),
        tensor_value,
    )


def pair_gradient(activations, cotangent, rows):
    tokens, width = activations.shape
    nz = lax.axis_size("z")
    pair_rows = rows * PAIR
    columns = activations.reshape(tokens, nz, pair_rows).transpose(1, 0, 2)
    columns = lax.all_to_all(columns, "z", 0, 0)
    cot_blocks = lax.all_gather(cotangent, "z")
    return jnp.einsum(
        "ktr,ktc->rc", columns, cot_blocks, preferred_element_type=jnp.float32
    )


def per_device(activations, cotangent, weight, momentum, step_index):
    rows = weight.shape[1]
    pair_sum = pair_gradient(activations, cotangent, rows)
    side = lax.axis_index("xh")
    own = lax.dynamic_slice_in_dim(pair_sum, side * rows, rows, 0)
    other = lax.dynamic_slice_in_dim(pair_sum, (1 - side) * rows, rows, 0)
    swapped = lax.ppermute(other.astype(jnp.bfloat16), "xh", [(0, 1), (1, 0)])
    gradient = own + swapped.astype(jnp.float32)
    momentum_new = (0.9 * momentum[0].astype(jnp.float32) + gradient).astype(jnp.bfloat16)
    half_step = (weight[0].astype(jnp.float32) - 0.5 * momentum_new.astype(jnp.float32)).astype(
        jnp.bfloat16
    )
    levels = lax.axis_size("rep").bit_length() - 1
    branches = [shifter(1 << bit_number) for bit_number in range(levels)]
    received = lax.switch(step_index[0] % levels, branches, half_step)
    averaged = (0.5 * (half_step.astype(jnp.float32) + received.astype(jnp.float32))).astype(
        jnp.bfloat16
    )
    return (averaged[None], momentum_new[None])


def solution(mesh):
    n_rep, n_shard = mesh.devices.shape
    split = Mesh(
        np.asarray(mesh.devices).reshape(n_rep, n_shard // PAIR, PAIR), ("rep", "z", "xh")
    )
    tokens = ("rep", "z", "xh")
    return jax.shard_map(
        per_device,
        mesh=split,
        in_specs=(
            P(tokens, None),
            P(tokens, None),
            P("rep", ("z", "xh"), None),
            P("rep", ("z", "xh"), None),
            P(),
        ),
        out_specs=(P("rep", ("z", "xh"), None), P("rep", ("z", "xh"), None)),
        check_vma=False,
    )
```

```python
import numpy as np
import jax
import jax.numpy as jnp
from jax import lax
from jax.sharding import Mesh, PartitionSpec as P

PAIR = 2
HALVES = 2


def from_behind(value, axis, by):
    count = lax.axis_size(axis)
    return lax.ppermute(value, axis, [(i, (i + by) % count) for i in range(count)])


def pair_gradient(activations, cotangent, rows):
    tokens, width = activations.shape
    nz = lax.axis_size("z")
    pair_rows = rows * PAIR
    columns = activations.reshape(tokens, nz, pair_rows).transpose(1, 0, 2)
    columns = lax.all_to_all(columns, "z", 0, 0)
    cot_blocks = lax.all_gather(cotangent, "z")
    return jnp.einsum(
        "ktr,ktc->rc", columns, cot_blocks, preferred_element_type=jnp.float32
    )


def tail(distance, halves):
    def run(own, other, weight, momentum):
        rows = own.shape[0]
        step = rows // halves
        averaged, momentum_new = [], []
        for lo in range(0, rows, step):
            swapped = lax.ppermute(other[lo : lo + step], "xh", [(0, 1), (1, 0)])
            gradient = own[lo : lo + step] + swapped.astype(jnp.float32)
            moment = (0.9 * momentum[lo : lo + step].astype(jnp.float32) + gradient).astype(
                jnp.bfloat16
            )
            half_step = (
                weight[lo : lo + step].astype(jnp.float32) - 0.5 * moment.astype(jnp.float32)
            ).astype(jnp.bfloat16)
            received = from_behind(half_step, "rep", distance)
            averaged.append(
                (0.5 * (half_step.astype(jnp.float32) + received.astype(jnp.float32))).astype(
                    jnp.bfloat16
                )
            )
            momentum_new.append(moment)
        return jnp.concatenate(averaged), jnp.concatenate(momentum_new)

    return run


def per_device(activations, cotangent, weight, momentum, step_index):
    rows = weight.shape[1]
    pair_sum = pair_gradient(activations, cotangent, rows)
    side = lax.axis_index("xh")
    own = lax.dynamic_slice_in_dim(pair_sum, side * rows, rows, 0)
    other = lax.dynamic_slice_in_dim(pair_sum, (1 - side) * rows, rows, 0).astype(jnp.bfloat16)
    levels = lax.axis_size("rep").bit_length() - 1
    branches = [tail(1 << bit_number, HALVES) for bit_number in range(levels)]
    averaged, momentum_new = lax.switch(
        step_index[0] % levels, branches, own, other, weight[0], momentum[0]
    )
    return (averaged[None], momentum_new[None])


def solution(mesh):
    n_rep, n_shard = mesh.devices.shape
    split = Mesh(
        np.asarray(mesh.devices).reshape(n_rep, n_shard // PAIR, PAIR), ("rep", "z", "xh")
    )
    tokens = ("rep", "z", "xh")
    return jax.shard_map(
        per_device,
        mesh=split,
        in_specs=(
            P(tokens, None),
            P(tokens, None),
            P("rep", ("z", "xh"), None),
            P("rep", ("z", "xh"), None),
            P(),
        ),
        out_specs=(P("rep", ("z", "xh"), None), P("rep", ("z", "xh"), None)),
        check_vma=False,
    )
```

```python
import numpy as np
import jax
import jax.numpy as jnp
from jax import lax
from jax.sharding import Mesh, PartitionSpec as P

PAIR = 2
HALVES = 2


def from_behind(value, axis, by):
    count = lax.axis_size(axis)
    return lax.ppermute(value, axis, [(i, (i + by) % count) for i in range(count)])


def pair_gradient(activations, cotangent, rows):
    tokens, width = activations.shape
    nz = lax.axis_size("z")
    pair_rows = rows * PAIR
    columns = activations.reshape(tokens, nz, pair_rows).transpose(1, 0, 2)
    columns = lax.all_to_all(columns, "z", 0, 0)
    cot_blocks = lax.all_gather(cotangent, "z")
    return jnp.einsum(
        "ktr,ktc->rc", columns, cot_blocks, preferred_element_type=jnp.float32
    )


def tail(distance, halves):
    def run(own, others, weight, momentum):
        rows = own.shape[0]
        step = rows // halves
        averaged, momentum_new = [], []
        for piece, lo in zip(others, range(0, rows, step)):
            swapped = lax.ppermute(piece, "xh", [(0, 1), (1, 0)])
            gradient = own[lo : lo + step] + swapped.astype(jnp.float32)
            moment = (0.9 * momentum[lo : lo + step].astype(jnp.float32) + gradient).astype(
                jnp.bfloat16
            )
            half_step = (
                weight[lo : lo + step].astype(jnp.float32) - 0.5 * moment.astype(jnp.float32)
            ).astype(jnp.bfloat16)
            received = from_behind(half_step, "rep", distance)
            averaged.append(
                (0.5 * (half_step.astype(jnp.float32) + received.astype(jnp.float32))).astype(
                    jnp.bfloat16
                )
            )
            momentum_new.append(moment)
        return jnp.concatenate(averaged), jnp.concatenate(momentum_new)

    return run


def per_device(activations, cotangent, weight, momentum, step_index):
    rows = weight.shape[1]
    pair_sum = pair_gradient(activations, cotangent, rows)
    side = lax.axis_index("xh")
    own = lax.dynamic_slice_in_dim(pair_sum, side * rows, rows, 0)
    step = rows // HALVES
    others = tuple(
        lax.dynamic_slice_in_dim(pair_sum, (1 - side) * rows + lo, step, 0).astype(jnp.bfloat16)
        for lo in range(0, rows, step)
    )
    levels = lax.axis_size("rep").bit_length() - 1
    branches = [tail(1 << bit_number, HALVES) for bit_number in range(levels)]
    averaged, momentum_new = lax.switch(
        step_index[0] % levels, branches, own, others, weight[0], momentum[0]
    )
    return (averaged[None], momentum_new[None])


def solution(mesh):
    n_rep, n_shard = mesh.devices.shape
    split = Mesh(
        np.asarray(mesh.devices).reshape(n_rep, n_shard // PAIR, PAIR), ("rep", "z", "xh")
    )
    tokens = ("rep", "z", "xh")
    return jax.shard_map(
        per_device,
        mesh=split,
        in_specs=(
            P(tokens, None),
            P(tokens, None),
            P("rep", ("z", "xh"), None),
            P("rep", ("z", "xh"), None),
            P(),
        ),
        out_specs=(P("rep", ("z", "xh"), None), P("rep", ("z", "xh"), None)),
        check_vma=False,
    )
```
